512 devices in a mesh: rep: 32 (over y, z_lo, core), row: 16 (over z_hi, x).
Axes of the slice: x: 4, y: 8, z: 8 (z_hi: 4, z_lo: 2; z = z_hi * 2 + z_lo), core: 2. Of those that a mesh axis runs over, the one named last changes fastest.
Arguments:
- features: bfloat16 [65536, 128], P(('rep', 'row')), may hold values from -6 to 6
- weight: bfloat16 [128, 256], replicated, may hold values from -0.5 to 0.5
- cotangent: bfloat16 [65536, 256], P(('rep', 'row')), may hold values from -6 to 6
- tile_values: bfloat16 [32, 16, 128, 128, 128], P('rep', 'row'), may hold values from -0.046875 to 0.046875
- tile_coords: int32 [32, 16, 128, 2], P('rep', 'row'), may hold values from 0 to 31, as said below
- tile_count: int32 [32, 16], P('rep', 'row'), may hold values from 32 to 128, as said below
Outputs:
- activated: bfloat16 [65536, 256], P(('rep', 'row'))
- feature_grad: bfloat16 [65536, 128], P(('rep', 'row'))
- weight_grad: float32 [128, 256], replicated
The draws below stay inside these ranges and needn't reach their ends.
Inputs may be any that keep to these rules, and one draw needn't show every extreme that they name: `tile_coords`: in each device's list the slots name distinct pairs; the first entry is a row tile below 32, the second a column tile below 16. `tile_count`: some device uses all 128 slots.
All inputs are finite; a program needn't handle non-finite values.
Results may differ from the reference program's by a relative error of at most 0.006.
Values may be sent and summed in bfloat16 or wider, within the bound.
No kernel may reach another device: no remote copies, remote signals or barrier semaphores. Data moves between devices by JAX's collectives and lax.ppermute only.
A program may use at most 64 MiB of HBM per device.

```python
import jax
import jax.numpy as jnp
from jax import lax

F_IN = 128
HIDDEN_SIZE = 256
TILE = 128
TILES_DEV = 128
VERTICES = 65536
N_REP = 32
N_ROW = 16


def draw_tile_count(key, part):
    lowest = max(1, TILES_DEV // 4)
    counts = jax.random.randint(jax.random.fold_in(key, 11), (N_REP, N_ROW), lowest, TILES_DEV + 1).astype(jnp.int32)
    full_row = jax.random.randint(jax.random.fold_in(key, 12), (), 0, N_ROW)
    return counts.at[0, full_row].set(TILES_DEV)


def draw_tile_coords(key, part):
    slot_total = N_REP * N_ROW
    key_list = jax.random.split(jax.random.fold_in(key, 13), N_REP * N_ROW)
    orders = jax.vmap(lambda sub_key: jax.random.permutation(sub_key, slot_total)[:TILES_DEV])(key_list)
    coords = jnp.stack([orders // N_ROW, orders % N_ROW], axis=-1).astype(jnp.int32)
    return coords.reshape(N_REP, N_ROW, TILES_DEV, 2)


def level_of(own_key, extent, shards, smallest, largest):
    level = 1.0
    for position, shards_of in shards:
        heights = jax.random.uniform(jax.random.fold_in(jax.random.fold_in(own_key, 6), position), (shards_of,), jnp.float32, smallest / len(shards), largest / len(shards))
        level = level * jnp.repeat(jnp.exp(heights), extent[position] // shards_of).reshape((-1,) + (1,) * (len(extent) - 1 - position))
    return level


def bell_draw(key, shape, spread, reach, pieces=(), held_as=jnp.bfloat16):
    drawn = spread * jax.random.normal(key, shape, jnp.float32)
    if pieces:
        drawn = drawn * level_of(key, shape, pieces, -0.22, 0.18)
    return jnp.clip(drawn, -reach, reach).astype(held_as)


def setup_inputs(seed: int = 0) -> dict:
    streams_of = jax.random.split(jax.random.key(seed), 7)
    return {
        "features": bell_draw(streams_of[0], (VERTICES, F_IN), 1.0, 6.0, ((0, 512),)),
        "weight": bell_draw(streams_of[1], (F_IN, HIDDEN_SIZE), F_IN ** -0.5, 0.5),
        "cotangent": bell_draw(streams_of[2], (VERTICES, HIDDEN_SIZE), 1.0, 6.0, ((0, 512),)),
        "tile_values": bell_draw(streams_of[3], (N_REP, N_ROW, TILES_DEV, TILE, TILE), (TILES_DEV * TILE) ** -0.5, 0.046875, ((0, 32), (1, 16))),
        "tile_coords": draw_tile_coords(jax.random.fold_in(streams_of[6], 71), 0),
        "tile_count": draw_tile_count(jax.random.fold_in(streams_of[6], 71), 0),
    }


def silu_slope(preactivation):
    sigmoid_value = jax.nn.sigmoid(preactivation)
    return sigmoid_value * (1.0 + preactivation * (1.0 - sigmoid_value))


def reference(features, weight, cotangent, tile_values, tile_coords, tile_count):
    feature_size = features.shape[1]
    blocks = features.reshape(N_REP, N_ROW, TILE, feature_size)
    slot_ids = jnp.arange(TILES_DEV, dtype=jnp.int32)
    rep_ids = jnp.arange(N_REP, dtype=jnp.int32)
    row_ids = jnp.arange(N_ROW, dtype=jnp.int32)
    device_ids = jnp.arange(N_REP * N_ROW, dtype=jnp.int32)

    def one_forward(running, index):
        rep_at = index // N_ROW
        row_at = index % N_ROW
        tile_block = tile_values[rep_at, row_at].astype(jnp.float32)
        coord_block = tile_coords[rep_at, row_at]
        live_mask = slot_ids < tile_count[rep_at, row_at]
        picked = jnp.take(blocks[rep_at], coord_block[:, 1], axis=0).astype(jnp.float32)
        product = jnp.einsum("tij,tjf->tif", tile_block, picked, precision=lax.Precision.HIGHEST)
        select = ((coord_block[:, 0][None, :] == rep_ids[:, None]) & live_mask[None, :]).astype(jnp.float32)
        partial_value = jnp.einsum("rt,tif->rif", select, product, precision=lax.Precision.HIGHEST)
        updated = lax.dynamic_index_in_dim(running, row_at, 1, keepdims=False) + partial_value
        return lax.dynamic_update_index_in_dim(running, updated, row_at, 1), None

    start_sum = jnp.zeros((N_REP, N_ROW, TILE, feature_size), jnp.float32)
    summed, _ = lax.scan(one_forward, start_sum, device_ids)
    aggregated = summed.reshape(N_REP * N_ROW * TILE, feature_size).astype(jnp.bfloat16)
    preactivation = jnp.dot(aggregated, weight, preferred_element_type=jnp.float32)
    activated = jax.nn.silu(preactivation).astype(jnp.bfloat16)
    grad_pre = (cotangent.astype(jnp.float32) * silu_slope(preactivation)).astype(jnp.bfloat16)
    grad_hidden = jnp.dot(grad_pre, weight.T, preferred_element_type=jnp.float32).astype(jnp.bfloat16)
    grad_blocks = grad_hidden.reshape(N_REP, N_ROW, TILE, feature_size)

    def one_backward(running, index):
        rep_at = index // N_ROW
        row_at = index % N_ROW
        tile_block = tile_values[rep_at, row_at].astype(jnp.float32)
        coord_block = tile_coords[rep_at, row_at]
        live_mask = slot_ids < tile_count[rep_at, row_at]
        row_grads = lax.dynamic_index_in_dim(grad_blocks, row_at, 1, keepdims=False)
        picked = jnp.take(row_grads, coord_block[:, 0], axis=0).astype(jnp.float32)
        product = jnp.einsum("tji,tjf->tif", tile_block, picked, precision=lax.Precision.HIGHEST)
        select = ((coord_block[:, 1][None, :] == row_ids[:, None]) & live_mask[None, :]).astype(jnp.float32)
        partial_value = jnp.einsum("ct,tif->cif", select, product, precision=lax.Precision.HIGHEST)
        return running.at[rep_at].add(partial_value), None

    back_sum, _ = lax.scan(one_backward, jnp.zeros((N_REP, N_ROW, TILE, feature_size), jnp.float32), device_ids)
    feature_grad = back_sum.reshape(N_REP * N_ROW * TILE, feature_size).astype(jnp.bfloat16)
    weight_grad = jnp.dot(aggregated.T, grad_pre, preferred_element_type=jnp.float32)
    return (activated, feature_grad, weight_grad)
```

```python
import math

import jax
import jax.numpy as jnp
from jax import lax
from jax.sharding import PartitionSpec as P


def silu_slope(preactivation):
    sigmoid_value = jax.nn.sigmoid(preactivation)
    return sigmoid_value * (1.0 + preactivation * (1.0 - sigmoid_value))


def tile_products(values, coords, live_count, sources, buckets, adjoint):
    slot_total = values.shape[0]
    tile_size = values.shape[1]
    width = sources.shape[2]
    group_size = math.gcd(slot_total, 32)
    round_total = (live_count + group_size - 1) // group_size
    bucket_ids = jnp.arange(buckets, dtype=jnp.int32)
    pick_column = 0 if adjoint else 1
    sum_column = 1 if adjoint else 0
    form = "tji,tjf->tif" if adjoint else "tij,tjf->tif"

    def advance(turn_index, running):
        begin_at = turn_index * group_size
        tile_block = lax.dynamic_slice_in_dim(values, begin_at, group_size, 0)
        coord_block = lax.dynamic_slice_in_dim(coords, begin_at, group_size, 0)
        live_mask = begin_at + jnp.arange(group_size, dtype=jnp.int32) < live_count
        picked = jnp.take(sources, coord_block[:, pick_column], axis=0)
        product = jnp.einsum(form, tile_block, picked, preferred_element_type=jnp.float32)
        select = (
            (coord_block[:, sum_column][None, :] == bucket_ids[:, None]) & live_mask[None, :]
        ).astype(jnp.float32)
        return running + jnp.einsum("rt,tif->rif", select, product, precision=lax.Precision.HIGHEST)

    start_sum = jnp.zeros((buckets, tile_size, width), jnp.float32)
    return lax.fori_loop(0, round_total, advance, start_sum)


def local(features, weight, cotangent, tile_values, tile_coords, tile_count):
    rep_count = lax.axis_size("rep")
    row_count = lax.axis_size("row")
    tile_size = features.shape[0]
    feature_size = features.shape[1]
    hidden_size = weight.shape[1]
    values = tile_values[0, 0]
    coords = tile_coords[0, 0]
    live_count = tile_count[0, 0]
    columns = lax.all_to_all(
        jnp.broadcast_to(features[None], (row_count, tile_size, feature_size)), "row", 0, 0, tiled=True
    )
    partial_rows = tile_products(values, coords, live_count, columns, rep_count, False)
    received = lax.all_to_all(partial_rows, "rep", 0, 0, tiled=True)
    aggregated = jnp.sum(received, axis=0).astype(jnp.bfloat16)
    preactivation = jnp.dot(aggregated, weight, preferred_element_type=jnp.float32)
    grad_pre = (cotangent.astype(jnp.float32) * silu_slope(preactivation)).astype(jnp.bfloat16)
    grad_hidden = lax.dot_general(
        grad_pre, weight, (((1,), (1,)), ((), ())), preferred_element_type=jnp.float32
    ).astype(jnp.bfloat16)
    grad_blocks = lax.all_to_all(
        jnp.broadcast_to(grad_hidden[None], (rep_count, tile_size, feature_size)), "rep", 0, 0, tiled=True
    )
    activated = jax.nn.silu(preactivation).astype(jnp.bfloat16)
    back_terms = tile_products(values, coords, live_count, grad_blocks, row_count, True)
    weight_term = lax.dot_general(
        aggregated, grad_pre, (((0,), (0,)), ((), ())), preferred_element_type=jnp.float32
    )
    chunk_rows = feature_size * hidden_size // (row_count * feature_size)
    weight_chunks = weight_term.reshape(row_count, chunk_rows, feature_size)
    outgoing = jnp.concatenate([back_terms, weight_chunks], axis=1)
    incoming = jnp.sum(lax.all_to_all(outgoing, "row", 0, 0, tiled=True), axis=0)
    feature_grad = incoming[:tile_size].astype(jnp.bfloat16)
    row_chunk = incoming[tile_size:]
    rep_summed = jnp.sum(
        lax.all_to_all(
            jnp.broadcast_to(row_chunk[None], (rep_count,) + row_chunk.shape), "rep", 0, 0, tiled=True
        ),
        axis=0,
    )
    weight_grad = lax.all_to_all(
        jnp.broadcast_to(rep_summed[None], (row_count,) + rep_summed.shape), "row", 0, 0, tiled=True
    ).reshape(feature_size, hidden_size)
    return (activated, feature_grad, weight_grad)


def solution(mesh):
    placed = (
        P(("rep", "row"), None),
        P(),
        P(("rep", "row"), None),
        P("rep", "row", None, None, None),
        P("rep", "row", None, None),
        P("rep", "row"),
    )
    return jax.shard_map(
        local,
        mesh=mesh,
        in_specs=placed,
        out_specs=(P(("rep", "row"), None), P(("rep", "row"), None), P()),
        check_vma=False,
    )
```

```python
import math

import jax
import jax.numpy as jnp
from jax import lax
from jax.experimental import pallas as pl
from jax.experimental.pallas import tpu as pltpu
from jax.sharding import PartitionSpec as P


SLOTS_STEP = 16


def silu_slope(preactivation):
    sigmoid_value = jax.nn.sigmoid(preactivation)
    return sigmoid_value * (1.0 + preactivation * (1.0 - sigmoid_value))


def tile_products(values, coords, live_count, sources, buckets, adjoint):
    slot_total, tile_size, _ = values.shape
    source_total, _, width = sources.shape
    step = math.gcd(slot_total, SLOTS_STEP)
    pick = 0 if adjoint else 1
    put = 1 if adjoint else 0
    flat_coords = coords.reshape(-1).astype(jnp.int32)
    live = jnp.reshape(live_count, (1,)).astype(jnp.int32)

    def kernel(coord_ref, live_ref, value_ref, source_ref, out_ref):
        first = pl.program_id(0) * step

        @pl.when(pl.program_id(0) == 0)
        def _():
            out_ref[...] = jnp.zeros_like(out_ref)

        def one(k, carry):
            slot = first + k

            @pl.when(slot < live_ref[0])
            def _():
                source_at = jnp.clip(coord_ref[2 * slot + pick], 0, source_total - 1)
                put_at = jnp.clip(coord_ref[2 * slot + put], 0, buckets - 1)
                tile = value_ref[k]
                source = source_ref[source_at]
                if adjoint:
                    product = lax.dot_general(
                        tile, source, (((0,), (0,)), ((), ())), preferred_element_type=jnp.float32
                    )
                else:
                    product = jnp.dot(tile, source, preferred_element_type=jnp.float32)
                out_ref[put_at] += product

            return carry

        lax.fori_loop(0, step, one, 0, unroll=True)

    def value_index(i, coord_ref, live_ref):
        last = jnp.maximum(live_ref[0] - 1, 0) // step
        return (jnp.minimum(i, last), 0, 0)

    grid_spec = pltpu.PrefetchScalarGridSpec(
        num_scalar_prefetch=2,
        grid=(slot_total // step,),
        in_specs=[
            pl.BlockSpec((step, tile_size, tile_size), value_index),
            pl.BlockSpec((source_total, tile_size, width), lambda i, c, l: (0, 0, 0)),
        ],
        out_specs=pl.BlockSpec((buckets, tile_size, width), lambda i, c, l: (0, 0, 0)),
    )
    return pl.pallas_call(
        kernel,
        grid_spec=grid_spec,
        out_shape=jax.ShapeDtypeStruct((buckets, tile_size, width), jnp.float32),
        compiler_params=pltpu.CompilerParams(dimension_semantics=("arbitrary",)),
    )(flat_coords, live, values, sources)


def local(features, weight, cotangent, tile_values, tile_coords, tile_count):
    rep_count = lax.axis_size("rep")
    row_count = lax.axis_size("row")
    tile_size = features.shape[0]
    feature_size = features.shape[1]
    hidden_size = weight.shape[1]
    values = tile_values[0, 0]
    coords = tile_coords[0, 0]
    live_count = tile_count[0, 0]
    columns = lax.all_to_all(
        jnp.broadcast_to(features[None], (row_count, tile_size, feature_size)), "row", 0, 0, tiled=True
    )
    partial_rows = tile_products(values, coords, live_count, columns, rep_count, False)
    received = lax.all_to_all(partial_rows, "rep", 0, 0, tiled=True)
    aggregated = jnp.sum(received, axis=0).astype(jnp.bfloat16)
    preactivation = jnp.dot(aggregated, weight, preferred_element_type=jnp.float32)
    grad_pre = (cotangent.astype(jnp.float32) * silu_slope(preactivation)).astype(jnp.bfloat16)
    grad_hidden = lax.dot_general(
        grad_pre, weight, (((1,), (1,)), ((), ())), preferred_element_type=jnp.float32
    ).astype(jnp.bfloat16)
    grad_blocks = lax.all_to_all(
        jnp.broadcast_to(grad_hidden[None], (rep_count, tile_size, feature_size)), "rep", 0, 0, tiled=True
    )
    activated = jax.nn.silu(preactivation).astype(jnp.bfloat16)
    back_terms = tile_products(values, coords, live_count, grad_blocks, row_count, True)
    weight_term = lax.dot_general(
        aggregated, grad_pre, (((0,), (0,)), ((), ())), preferred_element_type=jnp.float32
    )
    chunk_rows = feature_size * hidden_size // (row_count * feature_size)
    weight_chunks = weight_term.reshape(row_count, chunk_rows, feature_size)
    outgoing = jnp.concatenate([back_terms, weight_chunks], axis=1)
    incoming = jnp.sum(lax.all_to_all(outgoing, "row", 0, 0, tiled=True), axis=0)
    feature_grad = incoming[:tile_size].astype(jnp.bfloat16)
    row_chunk = incoming[tile_size:]
    rep_summed = jnp.sum(
        lax.all_to_all(
            jnp.broadcast_to(row_chunk[None], (rep_count,) + row_chunk.shape), "rep", 0, 0, tiled=True
        ),
        axis=0,
    )
    weight_grad = lax.all_to_all(
        jnp.broadcast_to(rep_summed[None], (row_count,) + rep_summed.shape), "row", 0, 0, tiled=True
    ).reshape(feature_size, hidden_size)
    return (activated, feature_grad, weight_grad)


def solution(mesh):
    placed = (
        P(("rep", "row"), None),
        P(),
        P(("rep", "row"), None),
        P("rep", "row", None, None, None),
        P("rep", "row", None, None),
        P("rep", "row"),
    )
    return jax.shard_map(
        local,
        mesh=mesh,
        in_specs=placed,
        out_specs=(P(("rep", "row"), None), P(("rep", "row"), None), P()),
        check_vma=False,
    )
```

```python
import math

import jax
import jax.numpy as jnp
from jax import lax
from jax.experimental import pallas as pl
from jax.experimental.pallas import tpu as pltpu
from jax.sharding import PartitionSpec as P


SLOTS_STEP = 32


def silu_slope(preactivation):
    sigmoid_value = jax.nn.sigmoid(preactivation)
    return sigmoid_value * (1.0 + preactivation * (1.0 - sigmoid_value))


def tile_products(values, coords, live_count, sources, buckets, adjoint):
    slot_total, tile_size, _ = values.shape
    source_total, _, width = sources.shape
    step = math.gcd(slot_total, SLOTS_STEP)
    pick = 0 if adjoint else 1
    put = 1 if adjoint else 0
    flat_coords = coords.reshape(-1).astype(jnp.int32)
    live = jnp.reshape(live_count, (1,)).astype(jnp.int32)

    def kernel(coord_ref, live_ref, value_ref, source_ref, out_ref):
        first = pl.program_id(0) * step

        @pl.when(pl.program_id(0) == 0)
        def _():
            out_ref[...] = jnp.zeros_like(out_ref)

        @pl.when(first < live_ref[0])
        def _():
            products = []
            for k in range(step):
                source_at = jnp.clip(coord_ref[2 * (first + k) + pick], 0, source_total - 1)
                tile = value_ref[k]
                source = source_ref[source_at]
                if adjoint:
                    product = lax.dot_general(
                        tile, source, (((0,), (0,)), ((), ())), preferred_element_type=jnp.float32
                    )
                else:
                    product = jnp.dot(tile, source, preferred_element_type=jnp.float32)
                products.append(product)
            for k in range(step):
                slot = first + k
                put_at = jnp.clip(coord_ref[2 * slot + put], 0, buckets - 1)
                kept = jnp.where(slot < live_ref[0], products[k], 0.0)
                out_ref[put_at] += kept

    def value_index(i, coord_ref, live_ref):
        last = jnp.maximum(live_ref[0] - 1, 0) // step
        return (jnp.minimum(i, last), 0, 0)

    grid_spec = pltpu.PrefetchScalarGridSpec(
        num_scalar_prefetch=2,
        grid=(slot_total // step,),
        in_specs=[
            pl.BlockSpec((step, tile_size, tile_size), value_index),
            pl.BlockSpec((source_total, tile_size, width), lambda i, c, l: (0, 0, 0)),
        ],
        out_specs=pl.BlockSpec((buckets, tile_size, width), lambda i, c, l: (0, 0, 0)),
    )
    return pl.pallas_call(
        kernel,
        grid_spec=grid_spec,
        out_shape=jax.ShapeDtypeStruct((buckets, tile_size, width), jnp.float32),
        compiler_params=pltpu.CompilerParams(dimension_semantics=("arbitrary",)),
    )(flat_coords, live, values, sources)


def local(features, weight, cotangent, tile_values, tile_coords, tile_count):
    rep_count = lax.axis_size("rep")
    row_count = lax.axis_size("row")
    tile_size = features.shape[0]
    feature_size = features.shape[1]
    hidden_size = weight.shape[1]
    values = tile_values[0, 0]
    coords = tile_coords[0, 0]
    live_count = tile_count[0, 0]
    columns = lax.all_to_all(
        jnp.broadcast_to(features[None], (row_count, tile_size, feature_size)), "row", 0, 0, tiled=True
    )
    partial_rows = tile_products(values, coords, live_count, columns, rep_count, False)
    received = lax.all_to_all(partial_rows, "rep", 0, 0, tiled=True)
    aggregated = jnp.sum(received, axis=0).astype(jnp.bfloat16)
    preactivation = jnp.dot(aggregated, weight, preferred_element_type=jnp.float32)
    grad_pre = (cotangent.astype(jnp.float32) * silu_slope(preactivation)).astype(jnp.bfloat16)
    grad_hidden = lax.dot_general(
        grad_pre, weight, (((1,), (1,)), ((), ())), preferred_element_type=jnp.float32
    ).astype(jnp.bfloat16)
    grad_blocks = lax.all_to_all(
        jnp.broadcast_to(grad_hidden[None], (rep_count, tile_size, feature_size)), "rep", 0, 0, tiled=True
    )
    activated = jax.nn.silu(preactivation).astype(jnp.bfloat16)
    back_terms = tile_products(values, coords, live_count, grad_blocks, row_count, True)
    weight_term = lax.dot_general(
        aggregated, grad_pre, (((0,), (0,)), ((), ())), preferred_element_type=jnp.float32
    )
    chunk_rows = feature_size * hidden_size // (row_count * feature_size)
    weight_chunks = weight_term.reshape(row_count, chunk_rows, feature_size)
    outgoing = jnp.concatenate([back_terms, weight_chunks], axis=1)
    incoming = jnp.sum(lax.all_to_all(outgoing, "row", 0, 0, tiled=True), axis=0)
    feature_grad = incoming[:tile_size].astype(jnp.bfloat16)
    row_chunk = incoming[tile_size:]
    rep_summed = jnp.sum(
        lax.all_to_all(
            jnp.broadcast_to(row_chunk[None], (rep_count,) + row_chunk.shape), "rep", 0, 0, tiled=True
        ),
        axis=0,
    )
    weight_grad = lax.all_to_all(
        jnp.broadcast_to(rep_summed[None], (row_count,) + rep_summed.shape), "row", 0, 0, tiled=True
    ).reshape(feature_size, hidden_size)
    return (activated, feature_grad, weight_grad)


def solution(mesh):
    placed = (
        P(("rep", "row"), None),
        P(),
        P(("rep", "row"), None),
        P("rep", "row", None, None, None),
        P("rep", "row", None, None),
        P("rep", "row"),
    )
    return jax.shard_map(
        local,
        mesh=mesh,
        in_specs=placed,
        out_specs=(P(("rep", "row"), None), P(("rep", "row"), None), P()),
        check_vma=False,
    )
```

```python
import math

import jax
import jax.numpy as jnp
from jax import lax
from jax.experimental import pallas as pl
from jax.experimental.pallas import tpu as pltpu
from jax.sharding import PartitionSpec as P


SLOTS_STEP = 32


def silu_slope(preactivation):
    sigmoid_value = jax.nn.sigmoid(preactivation)
    return sigmoid_value * (1.0 + preactivation * (1.0 - sigmoid_value))


def tile_products(values, coords, live_count, sources, buckets, adjoint):
    slot_total, tile_size, _ = values.shape
    source_total, _, width = sources.shape
    step = math.gcd(slot_total, SLOTS_STEP)
    pick = 0 if adjoint else 1
    put = 1 if adjoint else 0
    flat_coords = coords.reshape(-1).astype(jnp.int32)
    live = jnp.reshape(live_count, (1,)).astype(jnp.int32)

    def kernel(coord_ref, live_ref, value_ref, source_ref, out_ref):
        first = pl.program_id(0) * step

        @pl.when(pl.program_id(0) == 0)
        def _():
            out_ref[...] = jnp.zeros_like(out_ref)

        @pl.when(first < live_ref[0])
        def _():
            products = []
            for k in range(step):
                source_at = jnp.clip(coord_ref[2 * (first + k) + pick], 0, source_total - 1)
                tile = value_ref[k]
                source = source_ref[source_at]
                if adjoint:
                    product = lax.dot_general(
                        tile, source, (((0,), (0,)), ((), ())), preferred_element_type=jnp.float32
                    )
                else:
                    product = jnp.dot(tile, source, preferred_element_type=jnp.float32)
                products.append(product)
            for k in range(step):
                slot = first + k
                put_at = jnp.clip(coord_ref[2 * slot + put], 0, buckets - 1)
                kept = jnp.where(slot < live_ref[0], products[k], 0.0)
                out_ref[put_at] += kept

    def value_index(i, coord_ref, live_ref):
        last = jnp.maximum(live_ref[0] - 1, 0) // step
        return (jnp.minimum(i, last), 0, 0)

    grid_spec = pltpu.PrefetchScalarGridSpec(
        num_scalar_prefetch=2,
        grid=(slot_total // step,),
        in_specs=[
            pl.BlockSpec((step, tile_size, tile_size), value_index),
            pl.BlockSpec((source_total, tile_size, width), lambda i, c, l: (0, 0, 0)),
        ],
        out_specs=pl.BlockSpec((buckets, tile_size, width), lambda i, c, l: (0, 0, 0)),
    )
    return pl.pallas_call(
        kernel,
        grid_spec=grid_spec,
        out_shape=jax.ShapeDtypeStruct((buckets, tile_size, width), jnp.float32),
        compiler_params=pltpu.CompilerParams(dimension_semantics=("arbitrary",)),
    )(flat_coords, live, values, sources)


def local(features, weight, cotangent, tile_values, tile_coords, tile_count):
    rep_count = lax.axis_size("rep")
    row_count = lax.axis_size("row")
    tile_size = features.shape[0]
    feature_size = features.shape[1]
    hidden_size = weight.shape[1]
    values = tile_values[0, 0]
    coords = tile_coords[0, 0]
    live_count = tile_count[0, 0]
    columns = lax.all_to_all(
        jnp.broadcast_to(features[None], (row_count, tile_size, feature_size)), "row", 0, 0, tiled=True
    )
    partial_rows = tile_products(values, coords, live_count, columns, rep_count, False)
    received = lax.all_to_all(partial_rows.astype(jnp.bfloat16), "rep", 0, 0, tiled=True)
    aggregated = jnp.sum(received.astype(jnp.float32), axis=0).astype(jnp.bfloat16)
    preactivation = jnp.dot(aggregated, weight, preferred_element_type=jnp.float32)
    grad_pre = (cotangent.astype(jnp.float32) * silu_slope(preactivation)).astype(jnp.bfloat16)
    grad_hidden = lax.dot_general(
        grad_pre, weight, (((1,), (1,)), ((), ())), preferred_element_type=jnp.float32
    ).astype(jnp.bfloat16)
    grad_blocks = lax.all_to_all(
        jnp.broadcast_to(grad_hidden[None], (rep_count, tile_size, feature_size)), "rep", 0, 0, tiled=True
    )
    activated = jax.nn.silu(preactivation).astype(jnp.bfloat16)
    back_terms = tile_products(values, coords, live_count, grad_blocks, row_count, True)
    weight_term = lax.dot_general(
        aggregated, grad_pre, (((0,), (0,)), ((), ())), preferred_element_type=jnp.float32
    )
    chunk_rows = feature_size * hidden_size // (row_count * feature_size)
    weight_chunks = weight_term.reshape(row_count, chunk_rows, feature_size)
    outgoing = jnp.concatenate([back_terms, weight_chunks], axis=1)
    incoming = jnp.sum(lax.all_to_all(outgoing, "row", 0, 0, tiled=True), axis=0)
    feature_grad = incoming[:tile_size].astype(jnp.bfloat16)
    row_chunk = incoming[tile_size:]
    rep_summed = jnp.sum(
        lax.all_to_all(
            jnp.broadcast_to(row_chunk[None], (rep_count,) + row_chunk.shape), "rep", 0, 0, tiled=True
        ),
        axis=0,
    )
    weight_grad = lax.all_to_all(
        jnp.broadcast_to(rep_summed[None], (row_count,) + rep_summed.shape), "row", 0, 0, tiled=True
    ).reshape(feature_size, hidden_size)
    return (activated, feature_grad, weight_grad)


def solution(mesh):
    placed = (
        P(("rep", "row"), None),
        P(),
        P(("rep", "row"), None),
        P("rep", "row", None, None, None),
        P("rep", "row", None, None),
        P("rep", "row"),
    )
    return jax.shard_map(
        local,
        mesh=mesh,
        in_specs=placed,
        out_specs=(P(("rep", "row"), None), P(("rep", "row"), None), P()),
        check_vma=False,
    )
```

```python
import math

import jax
import jax.numpy as jnp
from jax import lax
from jax.experimental import pallas as pl
from jax.experimental.pallas import tpu as pltpu
from jax.sharding import PartitionSpec as P


SLOTS_STEP = 32


def silu_slope(preactivation):
    sigmoid_value = jax.nn.sigmoid(preactivation)
    return sigmoid_value * (1.0 + preactivation * (1.0 - sigmoid_value))


def tile_products(values, coords, live_count, sources, buckets, adjoint):
    slot_total, tile_size, _ = values.shape
    source_total, _, width = sources.shape
    step = math.gcd(slot_total, SLOTS_STEP)
    pick = 0 if adjoint else 1
    put = 1 if adjoint else 0
    flat_coords = coords.reshape(-1).astype(jnp.int32)
    live = jnp.reshape(live_count, (1,)).astype(jnp.int32)

    def kernel(coord_ref, live_ref, value_ref, source_ref, out_ref):
        first = pl.program_id(0) * step

        @pl.when(pl.program_id(0) == 0)
        def _():
            out_ref[...] = jnp.zeros_like(out_ref)

        @pl.when(first < live_ref[0])
        def _():
            products = []
            for k in range(step):
                source_at = jnp.clip(coord_ref[2 * (first + k) + pick], 0, source_total - 1)
                tile = value_ref[k]
                source = source_ref[source_at]
                if adjoint:
                    product = lax.dot_general(
                        tile, source, (((0,), (0,)), ((), ())), preferred_element_type=jnp.float32
                    )
                else:
                    product = jnp.dot(tile, source, preferred_element_type=jnp.float32)
                products.append(product)
            for k in range(step):
                slot = first + k
                put_at = jnp.clip(coord_ref[2 * slot + put], 0, buckets - 1)
                kept = jnp.where(slot < live_ref[0], products[k], 0.0)
                out_ref[put_at] += kept

    def value_index(i, coord_ref, live_ref):
        last = jnp.maximum(live_ref[0] - 1, 0) // step
        return (jnp.minimum(i, last), 0, 0)

    grid_spec = pltpu.PrefetchScalarGridSpec(
        num_scalar_prefetch=2,
        grid=(slot_total // step,),
        in_specs=[
            pl.BlockSpec((step, tile_size, tile_size), value_index),
            pl.BlockSpec((source_total, tile_size, width), lambda i, c, l: (0, 0, 0)),
        ],
        out_specs=pl.BlockSpec((buckets, tile_size, width), lambda i, c, l: (0, 0, 0)),
    )
    return pl.pallas_call(
        kernel,
        grid_spec=grid_spec,
        out_shape=jax.ShapeDtypeStruct((buckets, tile_size, width), jnp.float32),
        compiler_params=pltpu.CompilerParams(dimension_semantics=("arbitrary",)),
    )(flat_coords, live, values, sources)


def local(features, weight, cotangent, tile_values, tile_coords, tile_count):
    rep_count = lax.axis_size("rep")
    row_count = lax.axis_size("row")
    tile_size = features.shape[0]
    feature_size = features.shape[1]
    hidden_size = weight.shape[1]
    values = tile_values[0, 0]
    coords = tile_coords[0, 0]
    live_count = tile_count[0, 0]
    columns = lax.all_to_all(
        jnp.broadcast_to(features[None], (row_count, tile_size, feature_size)), "row", 0, 0, tiled=True
    )
    partial_rows = tile_products(values, coords, live_count, columns, rep_count, False)
    received = lax.all_to_all(partial_rows.astype(jnp.bfloat16), "rep", 0, 0, tiled=True)
    aggregated = jnp.sum(received.astype(jnp.float32), axis=0).astype(jnp.bfloat16)
    preactivation = jnp.dot(aggregated, weight, preferred_element_type=jnp.float32)
    grad_pre = (cotangent.astype(jnp.float32) * silu_slope(preactivation)).astype(jnp.bfloat16)
    grad_hidden = lax.dot_general(
        grad_pre, weight, (((1,), (1,)), ((), ())), preferred_element_type=jnp.float32
    ).astype(jnp.bfloat16)
    weight_term = lax.dot_general(
        aggregated, grad_pre, (((0,), (0,)), ((), ())), preferred_element_type=jnp.float32
    )
    chunk_rows = feature_size * hidden_size // (rep_count * feature_size)
    weight_chunks = weight_term.reshape(rep_count, chunk_rows, feature_size)
    weight_high = weight_chunks.astype(jnp.bfloat16)
    weight_low = (weight_chunks - weight_high.astype(jnp.float32)).astype(jnp.bfloat16)
    grad_outgoing = jnp.concatenate(
        [
            jnp.broadcast_to(grad_hidden[None], (rep_count, tile_size, feature_size)),
            weight_high,
            weight_low,
        ],
        axis=1,
    )
    grad_incoming = lax.all_to_all(grad_outgoing, "rep", 0, 0, tiled=True)
    grad_blocks = grad_incoming[:, :tile_size]
    rep_chunk = jnp.sum(
        grad_incoming[:, tile_size : tile_size + chunk_rows].astype(jnp.float32)
        + grad_incoming[:, tile_size + chunk_rows :].astype(jnp.float32),
        axis=0,
    )
    activated = jax.nn.silu(preactivation).astype(jnp.bfloat16)
    back_terms = tile_products(values, coords, live_count, grad_blocks, row_count, True)
    outgoing = jnp.concatenate(
        [back_terms, jnp.broadcast_to(rep_chunk[None], (row_count,) + rep_chunk.shape)], axis=1
    )
    incoming = jnp.sum(lax.all_to_all(outgoing, "row", 0, 0, tiled=True), axis=0)
    feature_grad = incoming[:tile_size].astype(jnp.bfloat16)
    weight_piece = incoming[tile_size:]
    weight_grad = lax.all_to_all(
        jnp.broadcast_to(weight_piece[None], (rep_count,) + weight_piece.shape), "rep", 0, 0, tiled=True
    ).reshape(feature_size, hidden_size)
    return (activated, feature_grad, weight_grad)


def solution(mesh):
    placed = (
        P(("rep", "row"), None),
        P(),
        P(("rep", "row"), None),
        P("rep", "row", None, None, None),
        P("rep", "row", None, None),
        P("rep", "row"),
    )
    return jax.shard_map(
        local,
        mesh=mesh,
        in_specs=placed,
        out_specs=(P(("rep", "row"), None), P(("rep", "row"), None), P()),
        check_vma=False,
    )
```

```python
import math

import jax
import jax.numpy as jnp
from jax import lax
from jax.experimental import pallas as pl
from jax.experimental.pallas import tpu as pltpu
from jax.sharding import PartitionSpec as P


SLOTS_STEP = 32


def silu_slope(preactivation):
    sigmoid_value = jax.nn.sigmoid(preactivation)
    return sigmoid_value * (1.0 + preactivation * (1.0 - sigmoid_value))


def tile_products(values, coords, live_count, sources, buckets, adjoint, out_dtype=jnp.float32, extra=None):
    slot_total, tile_size, _ = values.shape
    source_total, _, width = sources.shape
    step = math.gcd(slot_total, SLOTS_STEP)
    steps = slot_total // step
    pick = 0 if adjoint else 1
    put = 1 if adjoint else 0
    flat_coords = coords.reshape(-1).astype(jnp.int32)
    live = jnp.reshape(live_count, (1,)).astype(jnp.int32)
    extra_rows = 0 if extra is None else extra.shape[0]
    own_sum = out_dtype != jnp.float32

    def kernel(coord_ref, live_ref, value_ref, source_ref, *rest):
        if extra is None:
            out_ref, *scratch = rest
        else:
            extra_ref, out_ref, *scratch = rest
        sum_ref = scratch[0] if own_sum else out_ref
        first = pl.program_id(0) * step

        @pl.when(pl.program_id(0) == 0)
        def _():
            sum_ref[:, pl.ds(0, tile_size), :] = jnp.zeros((buckets, tile_size, width), jnp.float32)
            if extra is not None:
                out_ref[:, pl.ds(tile_size, extra_rows), :] = jnp.broadcast_to(
                    extra_ref[...][None], (buckets, extra_rows, width)
                )

        @pl.when(first < live_ref[0])
        def _():
            products = []
            for k in range(step):
                source_at = jnp.clip(coord_ref[2 * (first + k) + pick], 0, source_total - 1)
                tile = value_ref[k]
                source = source_ref[source_at]
                if adjoint:
                    product = lax.dot_general(
                        tile, source, (((0,), (0,)), ((), ())), preferred_element_type=jnp.float32
                    )
                else:
                    product = jnp.dot(tile, source, preferred_element_type=jnp.float32)
                products.append(product)
            for k in range(step):
                slot = first + k
                put_at = jnp.clip(coord_ref[2 * slot + put], 0, buckets - 1)
                kept = jnp.where(slot < live_ref[0], products[k], 0.0)
                sum_ref[put_at, pl.ds(0, tile_size), :] += kept

        if own_sum:

            @pl.when(pl.program_id(0) == steps - 1)
            def _():
                out_ref[...] = sum_ref[...].astype(out_dtype)

    def value_index(i, coord_ref, live_ref):
        last = jnp.maximum(live_ref[0] - 1, 0) // step
        return (jnp.minimum(i, last), 0, 0)

    in_specs = [
        pl.BlockSpec((step, tile_size, tile_size), value_index),
        pl.BlockSpec((source_total, tile_size, width), lambda i, c, l: (0, 0, 0)),
    ]
    operands = [flat_coords, live, values, sources]
    if extra is not None:
        in_specs.append(pl.BlockSpec((extra_rows, width), lambda i, c, l: (0, 0)))
        operands.append(extra)
    out_rows = tile_size + extra_rows
    grid_spec = pltpu.PrefetchScalarGridSpec(
        num_scalar_prefetch=2,
        grid=(steps,),
        in_specs=in_specs,
        out_specs=pl.BlockSpec((buckets, out_rows, width), lambda i, c, l: (0, 0, 0)),
        scratch_shapes=[pltpu.VMEM((buckets, tile_size, width), jnp.float32)] if own_sum else [],
    )
    return pl.pallas_call(
        kernel,
        grid_spec=grid_spec,
        out_shape=jax.ShapeDtypeStruct((buckets, out_rows, width), out_dtype),
        compiler_params=pltpu.CompilerParams(dimension_semantics=("arbitrary",)),
    )(*operands)


def local(features, weight, cotangent, tile_values, tile_coords, tile_count):
    rep_count = lax.axis_size("rep")
    row_count = lax.axis_size("row")
    tile_size = features.shape[0]
    feature_size = features.shape[1]
    hidden_size = weight.shape[1]
    values = tile_values[0, 0]
    coords = tile_coords[0, 0]
    live_count = tile_count[0, 0]
    columns = lax.all_to_all(
        jnp.broadcast_to(features[None], (row_count, tile_size, feature_size)), "row", 0, 0, tiled=True
    )
    partial_rows = tile_products(
        values, coords, live_count, columns, rep_count, False, out_dtype=jnp.bfloat16
    )
    received = lax.all_to_all(partial_rows, "rep", 0, 0, tiled=True)
    aggregated = jnp.sum(received.astype(jnp.float32), axis=0).astype(jnp.bfloat16)
    preactivation = jnp.dot(aggregated, weight, preferred_element_type=jnp.float32)
    grad_pre = (cotangent.astype(jnp.float32) * silu_slope(preactivation)).astype(jnp.bfloat16)
    grad_hidden = lax.dot_general(
        grad_pre, weight, (((1,), (1,)), ((), ())), preferred_element_type=jnp.float32
    ).astype(jnp.bfloat16)
    weight_term = lax.dot_general(
        aggregated, grad_pre, (((0,), (0,)), ((), ())), preferred_element_type=jnp.float32
    )
    chunk_rows = feature_size * hidden_size // (rep_count * feature_size)
    weight_chunks = weight_term.reshape(rep_count, chunk_rows, feature_size)
    weight_high = weight_chunks.astype(jnp.bfloat16)
    weight_low = (weight_chunks - weight_high.astype(jnp.float32)).astype(jnp.bfloat16)
    grad_outgoing = jnp.concatenate(
        [
            jnp.broadcast_to(grad_hidden[None], (rep_count, tile_size, feature_size)),
            weight_high,
            weight_low,
        ],
        axis=1,
    )
    grad_incoming = lax.all_to_all(grad_outgoing, "rep", 0, 0, tiled=True)
    rep_chunk = jnp.sum(
        grad_incoming[:, tile_size : tile_size + chunk_rows].astype(jnp.float32)
        + grad_incoming[:, tile_size + chunk_rows :].astype(jnp.float32),
        axis=0,
    )
    activated = jax.nn.silu(preactivation).astype(jnp.bfloat16)
    outgoing = tile_products(
        values, coords, live_count, grad_incoming, row_count, True, extra=rep_chunk
    )
    incoming = jnp.sum(lax.all_to_all(outgoing, "row", 0, 0, tiled=True), axis=0)
    feature_grad = incoming[:tile_size].astype(jnp.bfloat16)
    weight_piece = incoming[tile_size:]
    weight_grad = lax.all_to_all(
        jnp.broadcast_to(weight_piece[None], (rep_count,) + weight_piece.shape), "rep", 0, 0, tiled=True
    ).reshape(feature_size, hidden_size)
    return (activated, feature_grad, weight_grad)


def solution(mesh):
    placed = (
        P(("rep", "row"), None),
        P(),
        P(("rep", "row"), None),
        P("rep", "row", None, None, None),
        P("rep", "row", None, None),
        P("rep", "row"),
    )
    return jax.shard_map(
        local,
        mesh=mesh,
        in_specs=placed,
        out_specs=(P(("rep", "row"), None), P(("rep", "row"), None), P()),
        check_vma=False,
    )
```

```python
import math

import jax
import jax.numpy as jnp
from jax import lax
from jax.experimental import pallas as pl
from jax.experimental.pallas import tpu as pltpu
from jax.sharding import PartitionSpec as P


SLOTS_STEP = 64


def silu_slope(preactivation):
    sigmoid_value = jax.nn.sigmoid(preactivation)
    return sigmoid_value * (1.0 + preactivation * (1.0 - sigmoid_value))


def tile_products(values, coords, live_count, sources, buckets, adjoint, out_dtype=jnp.float32, extra=None):
    slot_total, tile_size, _ = values.shape
    source_total, _, width = sources.shape
    step = math.gcd(slot_total, SLOTS_STEP)
    steps = slot_total // step
    pick = 0 if adjoint else 1
    put = 1 if adjoint else 0
    flat_coords = coords.reshape(-1).astype(jnp.int32)
    live = jnp.reshape(live_count, (1,)).astype(jnp.int32)
    extra_rows = 0 if extra is None else extra.shape[0]
    own_sum = out_dtype != jnp.float32

    def kernel(coord_ref, live_ref, value_ref, source_ref, *rest):
        if extra is None:
            out_ref, *scratch = rest
        else:
            extra_ref, out_ref, *scratch = rest
        sum_ref = scratch[0] if own_sum else out_ref
        first = pl.program_id(0) * step

        @pl.when(pl.program_id(0) == 0)
        def _():
            sum_ref[:, pl.ds(0, tile_size), :] = jnp.zeros((buckets, tile_size, width), jnp.float32)
            if extra is not None:
                out_ref[:, pl.ds(tile_size, extra_rows), :] = jnp.broadcast_to(
                    extra_ref[...][None], (buckets, extra_rows, width)
                )

        @pl.when(first < live_ref[0])
        def _():
            products = []
            for k in range(step):
                source_at = jnp.clip(coord_ref[2 * (first + k) + pick], 0, source_total - 1)
                tile = value_ref[k]
                source = source_ref[source_at]
                if adjoint:
                    product = lax.dot_general(
                        tile, source, (((0,), (0,)), ((), ())), preferred_element_type=jnp.float32
                    )
                else:
                    product = jnp.dot(tile, source, preferred_element_type=jnp.float32)
                products.append(product)
            for k in range(step):
                slot = first + k
                put_at = jnp.clip(coord_ref[2 * slot + put], 0, buckets - 1)
                kept = jnp.where(slot < live_ref[0], products[k], 0.0)
                sum_ref[put_at, pl.ds(0, tile_size), :] += kept

        if own_sum:

            @pl.when(pl.program_id(0) == steps - 1)
            def _():
                out_ref[...] = sum_ref[...].astype(out_dtype)

    def value_index(i, coord_ref, live_ref):
        last = jnp.maximum(live_ref[0] - 1, 0) // step
        return (jnp.minimum(i, last), 0, 0)

    in_specs = [
        pl.BlockSpec((step, tile_size, tile_size), value_index),
        pl.BlockSpec((source_total, tile_size, width), lambda i, c, l: (0, 0, 0)),
    ]
    operands = [flat_coords, live, values, sources]
    if extra is not None:
        in_specs.append(pl.BlockSpec((extra_rows, width), lambda i, c, l: (0, 0)))
        operands.append(extra)
    out_rows = tile_size + extra_rows
    grid_spec = pltpu.PrefetchScalarGridSpec(
        num_scalar_prefetch=2,
        grid=(steps,),
        in_specs=in_specs,
        out_specs=pl.BlockSpec((buckets, out_rows, width), lambda i, c, l: (0, 0, 0)),
        scratch_shapes=[pltpu.VMEM((buckets, tile_size, width), jnp.float32)] if own_sum else [],
    )
    return pl.pallas_call(
        kernel,
        grid_spec=grid_spec,
        out_shape=jax.ShapeDtypeStruct((buckets, out_rows, width), out_dtype),
        compiler_params=pltpu.CompilerParams(dimension_semantics=("arbitrary",)),
    )(*operands)


def local(features, weight, cotangent, tile_values, tile_coords, tile_count):
    rep_count = lax.axis_size("rep")
    row_count = lax.axis_size("row")
    tile_size = features.shape[0]
    feature_size = features.shape[1]
    hidden_size = weight.shape[1]
    values = tile_values[0, 0]
    coords = tile_coords[0, 0]
    live_count = tile_count[0, 0]
    columns = lax.all_to_all(
        jnp.broadcast_to(features[None], (row_count, tile_size, feature_size)), "row", 0, 0, tiled=True
    )
    partial_rows = tile_products(
        values, coords, live_count, columns, rep_count, False, out_dtype=jnp.bfloat16
    )
    received = lax.all_to_all(partial_rows, "rep", 0, 0, tiled=True)
    aggregated = jnp.sum(received.astype(jnp.float32), axis=0).astype(jnp.bfloat16)
    preactivation = jnp.dot(aggregated, weight, preferred_element_type=jnp.float32)
    grad_pre = (cotangent.astype(jnp.float32) * silu_slope(preactivation)).astype(jnp.bfloat16)
    grad_hidden = lax.dot_general(
        grad_pre, weight, (((1,), (1,)), ((), ())), preferred_element_type=jnp.float32
    ).astype(jnp.bfloat16)
    weight_term = lax.dot_general(
        aggregated, grad_pre, (((0,), (0,)), ((), ())), preferred_element_type=jnp.float32
    )
    chunk_rows = feature_size * hidden_size // (rep_count * feature_size)
    weight_chunks = weight_term.reshape(rep_count, chunk_rows, feature_size)
    weight_high = weight_chunks.astype(jnp.bfloat16)
    weight_low = (weight_chunks - weight_high.astype(jnp.float32)).astype(jnp.bfloat16)
    grad_outgoing = jnp.concatenate(
        [
            jnp.broadcast_to(grad_hidden[None], (rep_count, tile_size, feature_size)),
            weight_high,
            weight_low,
        ],
        axis=1,
    )
    grad_incoming = lax.all_to_all(grad_outgoing, "rep", 0, 0, tiled=True)
    rep_chunk = jnp.sum(
        grad_incoming[:, tile_size : tile_size + chunk_rows].astype(jnp.float32)
        + grad_incoming[:, tile_size + chunk_rows :].astype(jnp.float32),
        axis=0,
    )
    activated = jax.nn.silu(preactivation).astype(jnp.bfloat16)
    outgoing = tile_products(
        values, coords, live_count, grad_incoming, row_count, True, extra=rep_chunk
    )
    incoming = jnp.sum(lax.all_to_all(outgoing, "row", 0, 0, tiled=True), axis=0)
    feature_grad = incoming[:tile_size].astype(jnp.bfloat16)
    weight_piece = incoming[tile_size:]
    weight_grad = lax.all_to_all(
        jnp.broadcast_to(weight_piece[None], (rep_count,) + weight_piece.shape), "rep", 0, 0, tiled=True
    ).reshape(feature_size, hidden_size)
    return (activated, feature_grad, weight_grad)


def solution(mesh):
    placed = (
        P(("rep", "row"), None),
        P(),
        P(("rep", "row"), None),
        P("rep", "row", None, None, None),
        P("rep", "row", None, None),
        P("rep", "row"),
    )
    return jax.shard_map(
        local,
        mesh=mesh,
        in_specs=placed,
        out_specs=(P(("rep", "row"), None), P(("rep", "row"), None), P()),
        check_vma=False,
    )
```

```python
import math

import jax
import jax.numpy as jnp
from jax import lax
from jax.experimental import pallas as pl
from jax.experimental.pallas import tpu as pltpu
from jax.sharding import PartitionSpec as P


SLOTS_STEP = 64


def silu_slope(preactivation):
    sigmoid_value = jax.nn.sigmoid(preactivation)
    return sigmoid_value * (1.0 + preactivation * (1.0 - sigmoid_value))


def tile_products(values, coords, live_count, sources, buckets, adjoint, out_dtype=jnp.float32, extra=None):
    slot_total, tile_size, _ = values.shape
    source_total, _, width = sources.shape
    step = math.gcd(slot_total, SLOTS_STEP)
    steps = slot_total // step
    pick = 0 if adjoint else 1
    put = 1 if adjoint else 0
    flat_coords = coords.reshape(-1).astype(jnp.int32)
    live = jnp.reshape(live_count, (1,)).astype(jnp.int32)
    extra_rows = 0 if extra is None else extra.shape[0]
    own_sum = out_dtype != jnp.float32

    def kernel(coord_ref, live_ref, value_ref, source_ref, *rest):
        if extra is None:
            out_ref, *scratch = rest
        else:
            extra_ref, out_ref, *scratch = rest
        sum_ref = scratch[0] if own_sum else out_ref
        first = pl.program_id(0) * step

        @pl.when(pl.program_id(0) == 0)
        def _():
            sum_ref[:, pl.ds(0, tile_size), :] = jnp.zeros((buckets, tile_size, width), jnp.float32)
            if extra is not None:
                out_ref[:, pl.ds(tile_size, extra_rows), :] = jnp.broadcast_to(
                    extra_ref[...][None], (buckets, extra_rows, width)
                )

        @pl.when(first < live_ref[0])
        def _():
            products = []
            for k in range(step):
                source_at = jnp.clip(coord_ref[2 * (first + k) + pick], 0, source_total - 1)
                tile = value_ref[k]
                source = source_ref[source_at]
                if adjoint:
                    product = lax.dot_general(
                        tile, source, (((0,), (0,)), ((), ())), preferred_element_type=jnp.float32
                    )
                else:
                    product = jnp.dot(tile, source, preferred_element_type=jnp.float32)
                products.append(product)
            for k in range(step):
                slot = first + k
                put_at = jnp.clip(coord_ref[2 * slot + put], 0, buckets - 1)
                kept = jnp.where(slot < live_ref[0], products[k], 0.0)
                sum_ref[put_at, pl.ds(0, tile_size), :] += kept

        if own_sum:

            @pl.when(pl.program_id(0) == steps - 1)
            def _():
                out_ref[...] = sum_ref[...].astype(out_dtype)

    def value_index(i, coord_ref, live_ref):
        last = jnp.maximum(live_ref[0] - 1, 0) // step
        return (jnp.minimum(i, last), 0, 0)

    in_specs = [
        pl.BlockSpec((step, tile_size, tile_size), value_index),
        pl.BlockSpec((source_total, tile_size, width), lambda i, c, l: (0, 0, 0)),
    ]
    operands = [flat_coords, live, values, sources]
    if extra is not None:
        in_specs.append(pl.BlockSpec((extra_rows, width), lambda i, c, l: (0, 0)))
        operands.append(extra)
    out_rows = tile_size + extra_rows
    grid_spec = pltpu.PrefetchScalarGridSpec(
        num_scalar_prefetch=2,
        grid=(steps,),
        in_specs=in_specs,
        out_specs=pl.BlockSpec((buckets, out_rows, width), lambda i, c, l: (0, 0, 0)),
        scratch_shapes=[pltpu.VMEM((buckets, tile_size, width), jnp.float32)] if own_sum else [],
    )
    return pl.pallas_call(
        kernel,
        grid_spec=grid_spec,
        out_shape=jax.ShapeDtypeStruct((buckets, out_rows, width), out_dtype),
        compiler_params=pltpu.CompilerParams(dimension_semantics=("arbitrary",)),
    )(*operands)


def local(features, weight, cotangent, tile_values, tile_coords, tile_count):
    rep_count = lax.axis_size("rep")
    row_count = lax.axis_size("row")
    tile_size = features.shape[0]
    feature_size = features.shape[1]
    hidden_size = weight.shape[1]
    values = tile_values[0, 0]
    coords = tile_coords[0, 0]
    live_count = tile_count[0, 0]
    columns = lax.all_to_all(
        jnp.broadcast_to(features[None], (row_count, tile_size, feature_size)), "row", 0, 0, tiled=True
    )
    partial_rows = tile_products(
        values, coords, live_count, columns, rep_count, False, out_dtype=jnp.bfloat16
    )
    received = lax.all_to_all(partial_rows, "rep", 0, 0, tiled=True)
    aggregated = jnp.sum(received.astype(jnp.float32), axis=0).astype(jnp.bfloat16)
    preactivation = jnp.dot(aggregated, weight, preferred_element_type=jnp.float32)
    grad_pre = (cotangent.astype(jnp.float32) * silu_slope(preactivation)).astype(jnp.bfloat16)
    grad_hidden = lax.dot_general(
        grad_pre, weight, (((1,), (1,)), ((), ())), preferred_element_type=jnp.float32
    ).astype(jnp.bfloat16)
    weight_term = lax.dot_general(
        aggregated, grad_pre, (((0,), (0,)), ((), ())), preferred_element_type=jnp.float32
    )
    chunk_rows = feature_size * hidden_size // (rep_count * feature_size)
    weight_chunks = weight_term.reshape(rep_count, chunk_rows, feature_size)
    weight_high = weight_chunks.astype(jnp.bfloat16)
    weight_low = (weight_chunks - weight_high.astype(jnp.float32)).astype(jnp.bfloat16)
    grad_outgoing = jnp.concatenate(
        [
            jnp.broadcast_to(grad_hidden[None], (rep_count, tile_size, feature_size)),
            weight_high,
            weight_low,
        ],
        axis=1,
    )
    grad_incoming = lax.all_to_all(grad_outgoing, "rep", 0, 0, tiled=True)
    rep_chunk = jnp.sum(
        grad_incoming[:, tile_size : tile_size + chunk_rows].astype(jnp.float32)
        + grad_incoming[:, tile_size + chunk_rows :].astype(jnp.float32),
        axis=0,
    )
    activated = jax.nn.silu(preactivation).astype(jnp.bfloat16)
    back_terms = tile_products(values, coords, live_count, grad_incoming, row_count, True)
    piece_high = rep_chunk.astype(jnp.bfloat16)
    piece_low = (rep_chunk - piece_high.astype(jnp.float32)).astype(jnp.bfloat16)
    outgoing = jnp.concatenate(
        [
            back_terms.astype(jnp.bfloat16),
            jnp.broadcast_to(piece_high[None], (row_count,) + piece_high.shape),
            jnp.broadcast_to(piece_low[None], (row_count,) + piece_low.shape),
        ],
        axis=1,
    )
    arrived = lax.all_to_all(outgoing, "row", 0, 0, tiled=True)
    feature_grad = jnp.sum(arrived[:, :tile_size].astype(jnp.float32), axis=0).astype(jnp.bfloat16)
    weight_piece = jnp.sum(
        arrived[:, tile_size : tile_size + chunk_rows].astype(jnp.float32)
        + arrived[:, tile_size + chunk_rows :].astype(jnp.float32),
        axis=0,
    )
    weight_grad = lax.all_to_all(
        jnp.broadcast_to(weight_piece[None], (rep_count,) + weight_piece.shape), "rep", 0, 0, tiled=True
    ).reshape(feature_size, hidden_size)
    return (activated, feature_grad, weight_grad)


def solution(mesh):
    placed = (
        P(("rep", "row"), None),
        P(),
        P(("rep", "row"), None),
        P("rep", "row", None, None, None),
        P("rep", "row", None, None),
        P("rep", "row"),
    )
    return jax.shard_map(
        local,
        mesh=mesh,
        in_specs=placed,
        out_specs=(P(("rep", "row"), None), P(("rep", "row"), None), P()),
        check_vma=False,
    )
```

```python
import math

import jax
import jax.numpy as jnp
from jax import lax
from jax.experimental import pallas as pl
from jax.experimental.pallas import tpu as pltpu
from jax.sharding import PartitionSpec as P


SLOTS_STEP = 64


def silu_slope(preactivation):
    sigmoid_value = jax.nn.sigmoid(preactivation)
    return sigmoid_value * (1.0 + preactivation * (1.0 - sigmoid_value))


def tile_products(values, coords, live_count, sources, buckets, adjoint, out_dtype=jnp.float32, pair_rows=0):
    slot_total, tile_size, _ = values.shape
    source_total, _, width = sources.shape
    step = math.gcd(slot_total, SLOTS_STEP)
    steps = slot_total // step
    pick = 0 if adjoint else 1
    put = 1 if adjoint else 0
    flat_coords = coords.reshape(-1).astype(jnp.int32)
    live = jnp.reshape(live_count, (1,)).astype(jnp.int32)
    extra_rows = pair_rows
    source_rows = sources.shape[1]
    own_sum = out_dtype != jnp.float32

    def kernel(coord_ref, live_ref, value_ref, source_ref, *rest):
        out_ref, *scratch = rest
        sum_ref = scratch[0] if own_sum else out_ref
        first = pl.program_id(0) * step

        @pl.when(pl.program_id(0) == 0)
        def _():
            sum_ref[:, pl.ds(0, tile_size), :] = jnp.zeros((buckets, tile_size, width), jnp.float32)
            if pair_rows:
                paired = jnp.zeros((pair_rows, width), jnp.float32)
                for s in range(source_total):
                    high = source_ref[s, pl.ds(tile_size, pair_rows), :].astype(jnp.float32)
                    low = source_ref[s, pl.ds(tile_size + pair_rows, pair_rows), :].astype(jnp.float32)
                    paired = paired + (high + low)
                out_ref[:, pl.ds(tile_size, pair_rows), :] = jnp.broadcast_to(
                    paired[None], (buckets, pair_rows, width)
                )

        @pl.when(first < live_ref[0])
        def _():
            products = []
            for k in range(step):
                source_at = jnp.clip(coord_ref[2 * (first + k) + pick], 0, source_total - 1)
                tile = value_ref[k]
                source = source_ref[source_at, pl.ds(0, tile_size), :]
                if adjoint:
                    product = lax.dot_general(
                        tile, source, (((0,), (0,)), ((), ())), preferred_element_type=jnp.float32
                    )
                else:
                    product = jnp.dot(tile, source, preferred_element_type=jnp.float32)
                products.append(product)
            for k in range(step):
                slot = first + k
                put_at = jnp.clip(coord_ref[2 * slot + put], 0, buckets - 1)
                kept = jnp.where(slot < live_ref[0], products[k], 0.0)
                sum_ref[put_at, pl.ds(0, tile_size), :] += kept

        if own_sum:

            @pl.when(pl.program_id(0) == steps - 1)
            def _():
                out_ref[...] = sum_ref[...].astype(out_dtype)

    def value_index(i, coord_ref, live_ref):
        last = jnp.maximum(live_ref[0] - 1, 0) // step
        return (jnp.minimum(i, last), 0, 0)

    in_specs = [
        pl.BlockSpec((step, tile_size, tile_size), value_index),
        pl.BlockSpec((source_total, source_rows, width), lambda i, c, l: (0, 0, 0)),
    ]
    operands = [flat_coords, live, values, sources]
    out_rows = tile_size + extra_rows
    grid_spec = pltpu.PrefetchScalarGridSpec(
        num_scalar_prefetch=2,
        grid=(steps,),
        in_specs=in_specs,
        out_specs=pl.BlockSpec((buckets, out_rows, width), lambda i, c, l: (0, 0, 0)),
        scratch_shapes=[pltpu.VMEM((buckets, tile_size, width), jnp.float32)] if own_sum else [],
    )
    return pl.pallas_call(
        kernel,
        grid_spec=grid_spec,
        out_shape=jax.ShapeDtypeStruct((buckets, out_rows, width), out_dtype),
        compiler_params=pltpu.CompilerParams(dimension_semantics=("arbitrary",)),
    )(*operands)


def local(features, weight, cotangent, tile_values, tile_coords, tile_count):
    rep_count = lax.axis_size("rep")
    row_count = lax.axis_size("row")
    tile_size = features.shape[0]
    feature_size = features.shape[1]
    hidden_size = weight.shape[1]
    values = tile_values[0, 0]
    coords = tile_coords[0, 0]
    live_count = tile_count[0, 0]
    columns = lax.all_to_all(
        jnp.broadcast_to(features[None], (row_count, tile_size, feature_size)), "row", 0, 0, tiled=True
    )
    partial_rows = tile_products(
        values, coords, live_count, columns, rep_count, False, out_dtype=jnp.bfloat16
    )
    received = lax.all_to_all(partial_rows, "rep", 0, 0, tiled=True)
    aggregated = jnp.sum(received.astype(jnp.float32), axis=0).astype(jnp.bfloat16)
    preactivation = jnp.dot(aggregated, weight, preferred_element_type=jnp.float32)
    grad_pre = (cotangent.astype(jnp.float32) * silu_slope(preactivation)).astype(jnp.bfloat16)
    grad_hidden = lax.dot_general(
        grad_pre, weight, (((1,), (1,)), ((), ())), preferred_element_type=jnp.float32
    ).astype(jnp.bfloat16)
    weight_term = lax.dot_general(
        aggregated, grad_pre, (((0,), (0,)), ((), ())), preferred_element_type=jnp.float32
    )
    chunk_rows = feature_size * hidden_size // (rep_count * feature_size)
    weight_chunks = weight_term.reshape(rep_count, chunk_rows, feature_size)
    weight_high = weight_chunks.astype(jnp.bfloat16)
    weight_low = (weight_chunks - weight_high.astype(jnp.float32)).astype(jnp.bfloat16)
    grad_outgoing = jnp.concatenate(
        [
            jnp.broadcast_to(grad_hidden[None], (rep_count, tile_size, feature_size)),
            weight_high,
            weight_low,
        ],
        axis=1,
    )
    grad_incoming = lax.all_to_all(grad_outgoing, "rep", 0, 0, tiled=True)
    activated = jax.nn.silu(preactivation).astype(jnp.bfloat16)
    outgoing = tile_products(
        values, coords, live_count, grad_incoming, row_count, True, pair_rows=chunk_rows
    )
    incoming = jnp.sum(lax.all_to_all(outgoing, "row", 0, 0, tiled=True), axis=0)
    feature_grad = incoming[:tile_size].astype(jnp.bfloat16)
    weight_piece = incoming[tile_size:]
    weight_grad = lax.all_to_all(
        jnp.broadcast_to(weight_piece[None], (rep_count,) + weight_piece.shape), "rep", 0, 0, tiled=True
    ).reshape(feature_size, hidden_size)
    return (activated, feature_grad, weight_grad)


def solution(mesh):
    placed = (
        P(("rep", "row"), None),
        P(),
        P(("rep", "row"), None),
        P("rep", "row", None, None, None),
        P("rep", "row", None, None),
        P("rep", "row"),
    )
    return jax.shard_map(
        local,
        mesh=mesh,
        in_specs=placed,
        out_specs=(P(("rep", "row"), None), P(("rep", "row"), None), P()),
        check_vma=False,
    )
```

```python
import math

import jax
import jax.numpy as jnp
from jax import lax
from jax.experimental import pallas as pl
from jax.experimental.pallas import tpu as pltpu
from jax.sharding import PartitionSpec as P


SLOTS_STEP = 64


def silu_slope(preactivation):
    sigmoid_value = jax.nn.sigmoid(preactivation)
    return sigmoid_value * (1.0 + preactivation * (1.0 - sigmoid_value))


def tile_products(values, coords, live_count, sources, buckets, adjoint, out_dtype=jnp.float32, pair_rows=0):
    slot_total, tile_size, _ = values.shape
    source_total, _, width = sources.shape
    step = math.gcd(slot_total, SLOTS_STEP)
    steps = slot_total // step
    pick = 0 if adjoint else 1
    put = 1 if adjoint else 0
    flat_coords = coords.reshape(-1).astype(jnp.int32)
    live = jnp.reshape(live_count, (1,)).astype(jnp.int32)
    extra_rows = pair_rows
    source_rows = sources.shape[1]
    own_sum = out_dtype != jnp.float32

    def kernel(coord_ref, live_ref, value_ref, source_ref, *rest):
        out_ref, *scratch = rest
        sum_ref = scratch[0] if own_sum else out_ref
        first = pl.program_id(0) * step

        @pl.when(pl.program_id(0) == 0)
        def _():
            sum_ref[:, pl.ds(0, tile_size), :] = jnp.zeros((buckets, tile_size, width), jnp.float32)
            if pair_rows:
                paired = jnp.zeros((pair_rows, width), jnp.float32)
                for s in range(source_total):
                    high = source_ref[s, pl.ds(tile_size, pair_rows), :].astype(jnp.float32)
                    low = source_ref[s, pl.ds(tile_size + pair_rows, pair_rows), :].astype(jnp.float32)
                    paired = paired + (high + low)
                out_ref[:, pl.ds(tile_size, pair_rows), :] = jnp.broadcast_to(
                    paired[None], (buckets, pair_rows, width)
                )

        @pl.when(first < live_ref[0])
        def _():
            products = []
            for k in range(step):
                source_at = jnp.clip(coord_ref[2 * (first + k) + pick], 0, source_total - 1)
                tile = value_ref[k]
                source = source_ref[source_at, pl.ds(0, tile_size), :]
                if adjoint:
                    product = lax.dot_general(
                        tile, source, (((0,), (0,)), ((), ())), preferred_element_type=jnp.float32
                    )
                else:
                    product = jnp.dot(tile, source, preferred_element_type=jnp.float32)
                products.append(product)
            for k in range(step):
                slot = first + k
                put_at = jnp.clip(coord_ref[2 * slot + put], 0, buckets - 1)
                kept = jnp.where(slot < live_ref[0], products[k], 0.0)
                sum_ref[put_at, pl.ds(0, tile_size), :] += kept

        if own_sum:

            @pl.when(pl.program_id(0) == steps - 1)
            def _():
                out_ref[...] = sum_ref[...].astype(out_dtype)

    def value_index(i, coord_ref, live_ref):
        last = jnp.maximum(live_ref[0] - 1, 0) // step
        return (jnp.minimum(i, last), 0, 0)

    in_specs = [
        pl.BlockSpec((step, tile_size, tile_size), value_index),
        pl.BlockSpec((source_total, source_rows, width), lambda i, c, l: (0, 0, 0)),
    ]
    operands = [flat_coords, live, values, sources]
    out_rows = tile_size + extra_rows
    grid_spec = pltpu.PrefetchScalarGridSpec(
        num_scalar_prefetch=2,
        grid=(steps,),
        in_specs=in_specs,
        out_specs=pl.BlockSpec((buckets, out_rows, width), lambda i, c, l: (0, 0, 0)),
        scratch_shapes=[pltpu.VMEM((buckets, tile_size, width), jnp.float32)] if own_sum else [],
    )
    return pl.pallas_call(
        kernel,
        grid_spec=grid_spec,
        out_shape=jax.ShapeDtypeStruct((buckets, out_rows, width), out_dtype),
        compiler_params=pltpu.CompilerParams(dimension_semantics=("arbitrary",)),
    )(*operands)


def local(features, weight, cotangent, tile_values, tile_coords, tile_count):
    rep_count = lax.axis_size("rep")
    row_count = lax.axis_size("row")
    tile_size = features.shape[0]
    feature_size = features.shape[1]
    hidden_size = weight.shape[1]
    values = tile_values[0, 0]
    coords = tile_coords[0, 0]
    live_count = tile_count[0, 0]
    columns = lax.all_to_all(
        jnp.broadcast_to(features[None], (row_count, tile_size, feature_size)), "row", 0, 0, tiled=True
    )
    partial_rows = tile_products(
        values, coords, live_count, columns, rep_count, False, out_dtype=jnp.bfloat16
    )
    received = lax.all_to_all(partial_rows, "rep", 0, 0, tiled=True)
    aggregated = jnp.sum(received.astype(jnp.float32), axis=0).astype(jnp.bfloat16)
    preactivation = jnp.dot(aggregated, weight, preferred_element_type=jnp.float32)
    grad_pre = (cotangent.astype(jnp.float32) * silu_slope(preactivation)).astype(jnp.bfloat16)
    grad_hidden = lax.dot_general(
        grad_pre, weight, (((1,), (1,)), ((), ())), preferred_element_type=jnp.float32
    ).astype(jnp.bfloat16)
    weight_term = lax.dot_general(
        aggregated, grad_pre, (((0,), (0,)), ((), ())), preferred_element_type=jnp.float32
    )
    chunk_rows = feature_size * hidden_size // (rep_count * feature_size)
    row_tiles = feature_size // chunk_rows
    column_tiles = hidden_size // feature_size
    weight_chunks = (
        weight_term.reshape(row_tiles, chunk_rows, column_tiles, feature_size)
        .transpose(0, 2, 1, 3)
        .reshape(rep_count, chunk_rows, feature_size)
    )
    weight_high = weight_chunks.astype(jnp.bfloat16)
    weight_low = (weight_chunks - weight_high.astype(jnp.float32)).astype(jnp.bfloat16)
    grad_outgoing = jnp.concatenate(
        [
            jnp.broadcast_to(grad_hidden[None], (rep_count, tile_size, feature_size)),
            weight_high,
            weight_low,
        ],
        axis=1,
    )
    grad_incoming = lax.all_to_all(grad_outgoing, "rep", 0, 0, tiled=True)
    activated = jax.nn.silu(preactivation).astype(jnp.bfloat16)
    outgoing = tile_products(
        values, coords, live_count, grad_incoming, row_count, True, pair_rows=chunk_rows
    )
    incoming = jnp.sum(lax.all_to_all(outgoing, "row", 0, 0, tiled=True), axis=0)
    feature_grad = incoming[:tile_size].astype(jnp.bfloat16)
    weight_piece = incoming[tile_size:]
    weight_grad = lax.all_to_all(
        jnp.broadcast_to(weight_piece[None], (rep_count,) + weight_piece.shape), "rep", 0, 0, tiled=True
    )
    weight_grad = (
        weight_grad.reshape(row_tiles, column_tiles, chunk_rows, feature_size)
        .transpose(0, 2, 1, 3)
        .reshape(feature_size, hidden_size)
    )
    return (activated, feature_grad, weight_grad)


def solution(mesh):
    placed = (
        P(("rep", "row"), None),
        P(),
        P(("rep", "row"), None),
        P("rep", "row", None, None, None),
        P("rep", "row", None, None),
        P("rep", "row"),
    )
    return jax.shard_map(
        local,
        mesh=mesh,
        in_specs=placed,
        out_specs=(P(("rep", "row"), None), P(("rep", "row"), None), P()),
        check_vma=False,
    )
```

```python
import math

import jax
import jax.numpy as jnp
from jax import lax
from jax.experimental import pallas as pl
from jax.experimental.pallas import tpu as pltpu
from jax.sharding import PartitionSpec as P


SLOTS_STEP = 64


def silu_slope(preactivation):
    sigmoid_value = jax.nn.sigmoid(preactivation)
    return sigmoid_value * (1.0 + preactivation * (1.0 - sigmoid_value))


def tile_products(values, coords, live_count, sources, buckets, adjoint, out_dtype=jnp.float32, pair_rows=0):
    slot_total, tile_size, _ = values.shape
    source_total, _, width = sources.shape
    step = math.gcd(slot_total, SLOTS_STEP)
    steps = slot_total // step
    pick = 0 if adjoint else 1
    put = 1 if adjoint else 0
    flat_coords = coords.reshape(-1).astype(jnp.int32)
    live = jnp.reshape(live_count, (1,)).astype(jnp.int32)
    extra_rows = pair_rows
    source_rows = sources.shape[1]
    own_sum = out_dtype != jnp.float32

    def kernel(coord_ref, live_ref, value_ref, source_ref, *rest):
        out_ref, *scratch = rest
        sum_ref = scratch[0] if own_sum else out_ref
        first = pl.program_id(0) * step

        @pl.when(pl.program_id(0) == 0)
        def _():
            sum_ref[:, pl.ds(0, tile_size), :] = jnp.zeros((buckets, tile_size, width), jnp.float32)
            if pair_rows:
                paired = jnp.zeros((pair_rows, width), jnp.float32)
                for s in range(source_total):
                    high = source_ref[s, pl.ds(tile_size, pair_rows), :].astype(jnp.float32)
                    low = source_ref[s, pl.ds(tile_size + pair_rows, pair_rows), :].astype(jnp.float32)
                    paired = paired + (high + low)
                out_ref[:, pl.ds(tile_size, pair_rows), :] = jnp.broadcast_to(
                    paired[None], (buckets, pair_rows, width)
                )

        @pl.when(first < live_ref[0])
        def _():
            products = []
            for k in range(step):
                source_at = jnp.clip(coord_ref[2 * (first + k) + pick], 0, source_total - 1)
                tile = value_ref[k]
                source = source_ref[source_at, pl.ds(0, tile_size), :]
                if adjoint:
                    product = lax.dot_general(
                        tile, source, (((0,), (0,)), ((), ())), preferred_element_type=jnp.float32
                    )
                else:
                    product = jnp.dot(tile, source, preferred_element_type=jnp.float32)
                products.append(product)
            for k in range(step):
                slot = first + k
                put_at = jnp.clip(coord_ref[2 * slot + put], 0, buckets - 1)
                kept = jnp.where(slot < live_ref[0], products[k], 0.0)
                sum_ref[put_at, pl.ds(0, tile_size), :] += kept

        if own_sum:

            @pl.when(pl.program_id(0) == steps - 1)
            def _():
                out_ref[...] = sum_ref[...].astype(out_dtype)

    def value_index(i, coord_ref, live_ref):
        last = jnp.maximum(live_ref[0] - 1, 0) // step
        return (jnp.minimum(i, last), 0, 0)

    in_specs = [
        pl.BlockSpec((step, tile_size, tile_size), value_index),
        pl.BlockSpec((source_total, source_rows, width), lambda i, c, l: (0, 0, 0)),
    ]
    operands = [flat_coords, live, values, sources]
    out_rows = tile_size + extra_rows
    grid_spec = pltpu.PrefetchScalarGridSpec(
        num_scalar_prefetch=2,
        grid=(steps,),
        in_specs=in_specs,
        out_specs=pl.BlockSpec((buckets, out_rows, width), lambda i, c, l: (0, 0, 0)),
        scratch_shapes=[pltpu.VMEM((buckets, tile_size, width), jnp.float32)] if own_sum else [],
    )
    return pl.pallas_call(
        kernel,
        grid_spec=grid_spec,
        out_shape=jax.ShapeDtypeStruct((buckets, out_rows, width), out_dtype),
        compiler_params=pltpu.CompilerParams(dimension_semantics=("arbitrary",)),
    )(*operands)


def local(features, weight, cotangent, tile_values, tile_coords, tile_count):
    rep_count = lax.axis_size("rep")
    row_count = lax.axis_size("row")
    tile_size = features.shape[0]
    feature_size = features.shape[1]
    hidden_size = weight.shape[1]
    values = tile_values[0, 0]
    coords = tile_coords[0, 0]
    live_count = tile_count[0, 0]
    columns = lax.all_to_all(
        jnp.concatenate([features] * row_count, axis=0).reshape(row_count, tile_size, feature_size),
        "row",
        0,
        0,
        tiled=True,
    )
    partial_rows = tile_products(
        values, coords, live_count, columns, rep_count, False, out_dtype=jnp.bfloat16
    )
    received = lax.all_to_all(partial_rows, "rep", 0, 0, tiled=True)
    aggregated = jnp.sum(received.astype(jnp.float32), axis=0).astype(jnp.bfloat16)
    preactivation = jnp.dot(aggregated, weight, preferred_element_type=jnp.float32)
    grad_pre = (cotangent.astype(jnp.float32) * silu_slope(preactivation)).astype(jnp.bfloat16)
    grad_hidden = lax.dot_general(
        grad_pre, weight, (((1,), (1,)), ((), ())), preferred_element_type=jnp.float32
    ).astype(jnp.bfloat16)
    weight_term = lax.dot_general(
        aggregated, grad_pre, (((0,), (0,)), ((), ())), preferred_element_type=jnp.float32
    )
    chunk_rows = feature_size * hidden_size // (rep_count * feature_size)
    row_tiles = feature_size // chunk_rows
    column_tiles = hidden_size // feature_size
    weight_chunks = (
        weight_term.reshape(row_tiles, chunk_rows, column_tiles, feature_size)
        .transpose(0, 2, 1, 3)
        .reshape(rep_count, chunk_rows, feature_size)
    )
    weight_high = weight_chunks.astype(jnp.bfloat16)
    weight_low = (weight_chunks - weight_high.astype(jnp.float32)).astype(jnp.bfloat16)
    grad_outgoing = jnp.concatenate(
        [
            jnp.broadcast_to(grad_hidden[None], (rep_count, tile_size, feature_size)),
            weight_high,
            weight_low,
        ],
        axis=1,
    )
    grad_incoming = lax.all_to_all(grad_outgoing, "rep", 0, 0, tiled=True)
    activated = jax.nn.silu(preactivation).astype(jnp.bfloat16)
    outgoing = tile_products(
        values, coords, live_count, grad_incoming, row_count, True, pair_rows=chunk_rows
    )
    incoming = jnp.sum(lax.all_to_all(outgoing, "row", 0, 0, tiled=True), axis=0)
    feature_grad = incoming[:tile_size].astype(jnp.bfloat16)
    weight_piece = incoming[tile_size:]
    weight_grad = lax.all_to_all(
        jnp.broadcast_to(weight_piece[None], (rep_count,) + weight_piece.shape), "rep", 0, 0, tiled=True
    )
    weight_grad = (
        weight_grad.reshape(row_tiles, column_tiles, chunk_rows, feature_size)
        .transpose(0, 2, 1, 3)
        .reshape(feature_size, hidden_size)
    )
    return (activated, feature_grad, weight_grad)


def solution(mesh):
    placed = (
        P(("rep", "row"), None),
        P(),
        P(("rep", "row"), None),
        P("rep", "row", None, None, None),
        P("rep", "row", None, None),
        P("rep", "row"),
    )
    return jax.shard_map(
        local,
        mesh=mesh,
        in_specs=placed,
        out_specs=(P(("rep", "row"), None), P(("rep", "row"), None), P()),
        check_vma=False,
    )
```
